1024 devices in a mesh: chan: 32 (over z_lo, x), slab: 32 (over y, z_hi, core).
Axes of the slice: x: 4, y: 4, z: 32 (z_hi: 4, z_lo: 8; z = z_hi * 8 + z_lo), core: 2. Of those that a mesh axis runs over, the one named last changes fastest.
Arguments:
- inputs: bfloat16 [256, 32, 8, 128], P('chan', 'slab'), may hold values from -6 to 6
- weight: bfloat16 [256, 3, 3, 3, 256], P('chan'), may hold values from -0.078125 to 0.078125
- conv_bias: bfloat16 [256], P('chan'), may hold values from -3 to 3
- out_grad: bfloat16 [256, 32, 8, 128], P('chan', 'slab'), may hold values from -6 to 6
Outputs:
- activated: bfloat16 [256, 32, 8, 128], P('chan', 'slab')
- input_grad: bfloat16 [256, 32, 8, 128], P('chan', 'slab')
- weight_grad: float32 [256, 3, 3, 3, 256], P('chan')
- bias_grad: float32 [256], P('chan')
The draws below stay inside these ranges and needn't reach their ends.
All inputs are finite; a program needn't handle non-finite values.
Results may differ from the reference program's by a relative error of at most 0.006.
Values may be sent and summed in bfloat16 or wider, within the bound.
No kernel may reach another device: no remote copies, remote signals or barrier semaphores. Data moves between devices by JAX's collectives and lax.ppermute only.
A program may use at most 32 MiB of HBM per device.

```python
import jax
import jax.numpy as jnp
from jax import lax

C = 256
H = 8
WD = 128
Z = 32


def shard_levels(own_key, shape, split, low, top_value):
    loudness = 1.0
    for dim, blocks in split:
        heights = jax.random.uniform(jax.random.fold_in(jax.random.fold_in(own_key, 6), dim), (blocks,), jnp.float32, low / len(split), top_value / len(split))
        loudness = loudness * jnp.repeat(jnp.exp(heights), shape[dim] // blocks).reshape((-1,) + (1,) * (len(shape) - 1 - dim))
    return loudness


def centred(key, dims, width, most, pieces=(), dtype=jnp.bfloat16):
    values = width * jax.random.normal(key, dims, jnp.float32)
    if pieces:
        values = values * shard_levels(key, dims, pieces, -0.22, 0.18)
    return jnp.clip(values, -most, most).astype(dtype)


def setup_inputs(seed: int = 0) -> dict:
    splits = jax.random.split(jax.random.key(seed), 5)
    inputs = centred(splits[0], (C, Z, H, WD), 1.0, 6.0, ((0, 32), (1, 32)))
    weight = centred(splits[1], (C, 3, 3, 3, C), (27 * C) ** -0.5, 0.078125, ((0, 32),))
    conv_bias = centred(splits[2], (C,), 0.5, 3.0, ((0, 32),))
    out_grad = centred(splits[3], (C, Z, H, WD), 1.0, 6.0, ((0, 32), (1, 32)))
    return dict(inputs=inputs, weight=weight, conv_bias=conv_bias, out_grad=out_grad)


def silu_grad(values):
    sig = jax.nn.sigmoid(values)
    return sig * (1.0 + values * (1.0 - sig))

def reference(inputs, weight, conv_bias, out_grad):
    n_chan, n_depth, n_high, n_wide = inputs.shape
    voxels = n_depth * n_high * n_wide
    padded = jnp.pad(inputs, ((0, 0), (1, 1), (1, 1), (1, 1)))
    pre_sum = jnp.zeros((n_chan, voxels), jnp.float32)
    for depth_tap in range(3):
        for high_tap in range(3):
            for wide_tap in range(3):
                in_plane = padded[:, depth_tap:depth_tap + n_depth, high_tap:high_tap + n_high, wide_tap:wide_tap + n_wide].reshape(n_chan, voxels)
                pre_sum = pre_sum + jnp.dot(weight[:, depth_tap, high_tap, wide_tap, :], in_plane, preferred_element_type=jnp.float32)
    pre_sum = pre_sum + conv_bias.astype(jnp.float32)[:, None]
    activated = jax.nn.silu(pre_sum).astype(jnp.bfloat16).reshape(inputs.shape)
    slope = (out_grad.reshape(n_chan, voxels).astype(jnp.float32) * silu_grad(pre_sum)).astype(jnp.bfloat16)
    slope_pad = jnp.pad(slope.reshape(n_chan, n_depth, n_high, n_wide), ((0, 0), (1, 1), (1, 1), (1, 1)))
    back_sum = jnp.zeros((n_chan, voxels), jnp.float32)
    kernel_list = []
    for depth_tap in range(3):
        for high_tap in range(3):
            for wide_tap in range(3):
                in_plane = padded[:, depth_tap:depth_tap + n_depth, high_tap:high_tap + n_high, wide_tap:wide_tap + n_wide].reshape(n_chan, voxels)
                kernel_list.append(lax.dot_general(slope, in_plane, (((1,), (1,)), ((), ())), preferred_element_type=jnp.float32))
                back_slab = slope_pad[:, 2 - depth_tap:2 - depth_tap + n_depth, 2 - high_tap:2 - high_tap + n_high, 2 - wide_tap:2 - wide_tap + n_wide].reshape(n_chan, voxels)
                back_sum = back_sum + lax.dot_general(weight[:, depth_tap, high_tap, wide_tap, :], back_slab, (((0,), (0,)), ((), ())), preferred_element_type=jnp.float32)
    grad_scale = 1.0 / jnp.sqrt(jnp.float32(voxels))
    weight_grad = jnp.stack(kernel_list, axis=1).reshape(n_chan, 3, 3, 3, n_chan) * grad_scale
    bias_grad = lax.optimization_barrier(jnp.sum(slope.astype(jnp.float32), axis=1)) * grad_scale
    input_grad = back_sum.astype(jnp.bfloat16).reshape(inputs.shape)
    return (activated, input_grad, weight_grad, bias_grad)
```

```python
import math

import jax
import jax.numpy as jnp
from jax import lax
from jax.sharding import PartitionSpec as P


def silu_grad(values):
    sig = jax.nn.sigmoid(values)
    return sig * (1.0 + values * (1.0 - sig))


def shifted_cells(values, high_step, wide_step, n_high, n_wide):
    length = values.shape[-1]
    offset = high_step * n_wide + wide_step
    if offset > 0:
        filler = jnp.zeros(values.shape[:-1] + (offset,), values.dtype)
        moved = jnp.concatenate([values[..., offset:], filler], axis=-1)
    elif offset < 0:
        filler = jnp.zeros(values.shape[:-1] + (-offset,), values.dtype)
        moved = jnp.concatenate([filler, values[..., :offset]], axis=-1)
    else:
        moved = values
    position = lax.iota(jnp.int32, length)
    high_index = position // n_wide % n_high + high_step
    wide_index = position % n_wide + wide_step
    valid = (high_index >= 0) & (high_index < n_high) & (wide_index >= 0) & (wide_index < n_wide)
    return jnp.where(valid, moved, jnp.zeros_like(moved))


def from_below(values, axis):
    count = lax.axis_size(axis)
    return lax.ppermute(values, axis, [(i, i + 1) for i in range(count - 1)])


def from_above(values, axis):
    count = lax.axis_size(axis)
    return lax.ppermute(values, axis, [(i + 1, i) for i in range(count - 1)])


def tap_sums(products, sign, n_high, n_wide):
    sums = []
    for depth_tap in range(3):
        total = None
        for high_tap in range(3):
            for wide_tap in range(3):
                moved = shifted_cells(
                    products[depth_tap, high_tap, wide_tap],
                    sign * (high_tap - 1),
                    sign * (wide_tap - 1),
                    n_high,
                    n_wide,
                )
                total = moved if total is None else total + moved
        sums.append(total)
    return sums


def on_device(inputs, weight, conv_bias, out_grad):
    n_local, n_depth, n_high, n_wide = inputs.shape
    n_chan = weight.shape[4]
    cells = n_depth * n_high * n_wide
    grad_scale = 1.0 / math.sqrt(cells * lax.axis_size("slab"))

    weight_flat = weight.reshape(n_local, 27, n_chan)
    weight_cols = lax.all_to_all(weight_flat, "chan", split_axis=2, concat_axis=0, tiled=True)

    in_flat = inputs.reshape(n_local, cells)
    in_all = lax.all_gather(in_flat, "chan", axis=0, tiled=True)
    weight_rows = weight_flat.transpose(1, 0, 2).reshape(27 * n_local, n_chan)
    products = jnp.dot(weight_rows, in_all, preferred_element_type=jnp.float32)
    products = products.reshape(3, 3, 3, n_local, cells)
    fwd = tap_sums(products, 1, n_high, n_wide)
    pre_sum = fwd[1] + from_below(fwd[0], "slab") + from_above(fwd[2], "slab")
    pre_sum = pre_sum + conv_bias.astype(jnp.float32)[:, None]
    activated = jax.nn.silu(pre_sum).astype(jnp.bfloat16).reshape(inputs.shape)
    slope = (out_grad.reshape(n_local, cells).astype(jnp.float32) * silu_grad(pre_sum)).astype(
        jnp.bfloat16
    )

    slope_below = from_below(slope, "slab")
    slope_above = from_above(slope, "slab")
    slope_planes = (slope_above, slope, slope_below)
    slope_moved = jnp.stack(
        [
            shifted_cells(slope_planes[depth_tap], 1 - high_tap, 1 - wide_tap, n_high, n_wide)
            for depth_tap in range(3)
            for high_tap in range(3)
            for wide_tap in range(3)
        ],
        axis=0,
    ).reshape(27 * n_local, cells)
    tap_grad = lax.dot_general(
        slope_moved, in_all, (((1,), (1,)), ((), ())), preferred_element_type=jnp.float32
    )
    kernel_part = tap_grad.reshape(27, n_local, n_chan).transpose(1, 0, 2)
    bias_part = jnp.sum(slope.astype(jnp.float32), axis=1)
    bias_row = jnp.zeros((n_local, 1, n_chan), jnp.float32).at[:, 0, 0].set(bias_part)
    both = jnp.concatenate([kernel_part, bias_row], axis=1)
    n_slab = lax.axis_size("slab")
    pieces = lax.all_to_all(both.reshape(n_slab, -1), "slab", split_axis=0, concat_axis=0, tiled=True)
    summed = jnp.sum(pieces, axis=0, keepdims=True)
    total = lax.all_gather(summed, "slab", axis=0, tiled=True).reshape(n_local, 28, n_chan)
    kernel_total = total[:, :27].reshape(n_local, 3, 3, 3, n_chan) * grad_scale
    bias_total = total[:, 27, 0] * grad_scale

    slope_all = lax.all_gather(slope, "chan", axis=0, tiled=True)
    back = lax.dot_general(
        weight_cols.reshape(n_chan, 27 * n_local),
        slope_all,
        (((0,), (0,)), ((), ())),
        preferred_element_type=jnp.float32,
    )
    back = back.reshape(3, 3, 3, n_local, cells)
    bwd = tap_sums(back, -1, n_high, n_wide)
    back_total = bwd[1] + from_above(bwd[0], "slab") + from_below(bwd[2], "slab")
    input_grad = back_total.astype(jnp.bfloat16).reshape(inputs.shape)
    return (activated, input_grad, kernel_total, bias_total)


def solution(mesh):
    placed = (
        P("chan", "slab", None, None),
        P("chan", None, None, None, None),
        P("chan"),
        P("chan", "slab", None, None),
    )
    return jax.shard_map(
        on_device,
        mesh=mesh,
        in_specs=placed,
        out_specs=(
            P("chan", "slab", None, None),
            P("chan", "slab", None, None),
            P("chan", None, None, None, None),
            P("chan"),
        ),
        check_vma=False,
    )
```

```python
import math

import jax
import jax.numpy as jnp
from jax import lax
from jax.sharding import PartitionSpec as P


def silu_grad(values):
    sig = jax.nn.sigmoid(values)
    return sig * (1.0 + values * (1.0 - sig))


def shifted_cells(values, high_step, wide_step, n_high, n_wide):
    length = values.shape[-1]
    offset = high_step * n_wide + wide_step
    if offset > 0:
        filler = jnp.zeros(values.shape[:-1] + (offset,), values.dtype)
        moved = jnp.concatenate([values[..., offset:], filler], axis=-1)
    elif offset < 0:
        filler = jnp.zeros(values.shape[:-1] + (-offset,), values.dtype)
        moved = jnp.concatenate([filler, values[..., :offset]], axis=-1)
    else:
        moved = values
    position = lax.iota(jnp.int32, length)
    high_index = position // n_wide % n_high + high_step
    wide_index = position % n_wide + wide_step
    valid = (high_index >= 0) & (high_index < n_high) & (wide_index >= 0) & (wide_index < n_wide)
    return jnp.where(valid, moved, jnp.zeros_like(moved))


def from_below(values, axis):
    count = lax.axis_size(axis)
    return lax.ppermute(values, axis, [(i, i + 1) for i in range(count - 1)])


def from_above(values, axis):
    count = lax.axis_size(axis)
    return lax.ppermute(values, axis, [(i + 1, i) for i in range(count - 1)])


def gathered(values, axis):
    count = lax.axis_size(axis)
    copies = jnp.broadcast_to(values[None], (count, *values.shape))
    blocks = lax.all_to_all(copies, axis, split_axis=0, concat_axis=0, tiled=True)
    return blocks.reshape(count * values.shape[0], *values.shape[1:])


def tap_sums(products, sign, n_high, n_wide):
    sums = []
    for depth_tap in range(3):
        total = None
        for high_tap in range(3):
            for wide_tap in range(3):
                moved = shifted_cells(
                    products[depth_tap, high_tap, wide_tap],
                    sign * (high_tap - 1),
                    sign * (wide_tap - 1),
                    n_high,
                    n_wide,
                )
                total = moved if total is None else total + moved
        sums.append(total)
    return sums


def on_device(inputs, weight, conv_bias, out_grad):
    n_local, n_depth, n_high, n_wide = inputs.shape
    n_chan = weight.shape[4]
    cells = n_depth * n_high * n_wide
    grad_scale = 1.0 / math.sqrt(cells * lax.axis_size("slab"))

    weight_flat = weight.reshape(n_local, 27, n_chan)
    weight_cols = lax.all_to_all(weight_flat, "chan", split_axis=2, concat_axis=0, tiled=True)

    in_flat = inputs.reshape(n_local, cells)
    in_all = gathered(in_flat, "chan")
    weight_rows = weight_flat.transpose(1, 0, 2).reshape(27 * n_local, n_chan)
    products = jnp.dot(weight_rows, in_all, preferred_element_type=jnp.float32)
    products = products.reshape(3, 3, 3, n_local, cells)
    fwd = tap_sums(products, 1, n_high, n_wide)
    pre_sum = fwd[1] + from_below(fwd[0], "slab") + from_above(fwd[2], "slab")
    pre_sum = pre_sum + conv_bias.astype(jnp.float32)[:, None]
    activated = jax.nn.silu(pre_sum).astype(jnp.bfloat16).reshape(inputs.shape)
    slope = (out_grad.reshape(n_local, cells).astype(jnp.float32) * silu_grad(pre_sum)).astype(
        jnp.bfloat16
    )

    slope_below = from_below(slope, "slab")
    slope_above = from_above(slope, "slab")
    slope_planes = (slope_above, slope, slope_below)
    slope_moved = jnp.stack(
        [
            shifted_cells(slope_planes[depth_tap], 1 - high_tap, 1 - wide_tap, n_high, n_wide)
            for depth_tap in range(3)
            for high_tap in range(3)
            for wide_tap in range(3)
        ],
        axis=0,
    ).reshape(27 * n_local, cells)
    tap_grad = lax.dot_general(
        slope_moved, in_all, (((1,), (1,)), ((), ())), preferred_element_type=jnp.float32
    )
    kernel_part = tap_grad.reshape(27, n_local, n_chan).transpose(1, 0, 2)
    bias_part = jnp.sum(slope.astype(jnp.float32), axis=1)
    bias_row = jnp.zeros((n_local, 1, n_chan), jnp.float32).at[:, 0, 0].set(bias_part)
    both = jnp.concatenate([kernel_part, bias_row], axis=1)
    n_slab = lax.axis_size("slab")
    pieces = lax.all_to_all(both.reshape(n_slab, -1), "slab", split_axis=0, concat_axis=0, tiled=True)
    summed = jnp.sum(pieces, axis=0, keepdims=True)
    total = gathered(summed, "slab").reshape(n_local, 28, n_chan)
    kernel_total = total[:, :27].reshape(n_local, 3, 3, 3, n_chan) * grad_scale
    bias_total = total[:, 27, 0] * grad_scale

    slope_all = gathered(slope, "chan")
    back = lax.dot_general(
        weight_cols.reshape(n_chan, 27 * n_local),
        slope_all,
        (((0,), (0,)), ((), ())),
        preferred_element_type=jnp.float32,
    )
    back = back.reshape(3, 3, 3, n_local, cells)
    bwd = tap_sums(back, -1, n_high, n_wide)
    back_total = bwd[1] + from_above(bwd[0], "slab") + from_below(bwd[2], "slab")
    input_grad = back_total.astype(jnp.bfloat16).reshape(inputs.shape)
    return (activated, input_grad, kernel_total, bias_total)


def solution(mesh):
    placed = (
        P("chan", "slab", None, None),
        P("chan", None, None, None, None),
        P("chan"),
        P("chan", "slab", None, None),
    )
    return jax.shard_map(
        on_device,
        mesh=mesh,
        in_specs=placed,
        out_specs=(
            P("chan", "slab", None, None),
            P("chan", "slab", None, None),
            P("chan", None, None, None, None),
            P("chan"),
        ),
        check_vma=False,
    )
```

```python
import math

import jax
import jax.numpy as jnp
from jax import lax
from jax.sharding import PartitionSpec as P


def silu_grad(values):
    sig = jax.nn.sigmoid(values)
    return sig * (1.0 + values * (1.0 - sig))


def shifted_cells(values, high_step, wide_step, n_high, n_wide):
    length = values.shape[-1]
    offset = high_step * n_wide + wide_step
    if offset > 0:
        filler = jnp.zeros(values.shape[:-1] + (offset,), values.dtype)
        moved = jnp.concatenate([values[..., offset:], filler], axis=-1)
    elif offset < 0:
        filler = jnp.zeros(values.shape[:-1] + (-offset,), values.dtype)
        moved = jnp.concatenate([filler, values[..., :offset]], axis=-1)
    else:
        moved = values
    position = lax.iota(jnp.int32, length)
    high_index = position // n_wide % n_high + high_step
    wide_index = position % n_wide + wide_step
    valid = (high_index >= 0) & (high_index < n_high) & (wide_index >= 0) & (wide_index < n_wide)
    return jnp.where(valid, moved, jnp.zeros_like(moved))


def from_below(values, axis):
    count = lax.axis_size(axis)
    return lax.ppermute(values, axis, [(i, i + 1) for i in range(count - 1)])


def from_above(values, axis):
    count = lax.axis_size(axis)
    return lax.ppermute(values, axis, [(i + 1, i) for i in range(count - 1)])


def gathered(values, axis):
    count = lax.axis_size(axis)
    copies = jnp.broadcast_to(values[None], (count, *values.shape))
    blocks = lax.all_to_all(copies, axis, split_axis=0, concat_axis=0, tiled=True)
    return blocks.reshape(count * values.shape[0], *values.shape[1:])


REDUCE = "pair"


def slab_total(both):
    n_slab = lax.axis_size("slab")
    if REDUCE == "psum":
        return lax.psum(both, "slab")
    if REDUCE == "rs_ag":
        piece = lax.psum_scatter(both.reshape(n_slab, -1), "slab", scatter_dimension=0, tiled=True)
        return lax.all_gather(piece, "slab", axis=0, tiled=True).reshape(both.shape)
    if REDUCE == "rs_a2a":
        piece = lax.psum_scatter(both.reshape(n_slab, -1), "slab", scatter_dimension=0, tiled=True)
        return gathered(piece, "slab").reshape(both.shape)
    if REDUCE == "pair":
        halves = both.reshape(2, n_slab, -1)
        parity = lax.axis_index("slab") % 2
        keep = jnp.where(parity == 0, halves[0], halves[1])
        give = jnp.where(parity == 0, halves[1], halves[0])
        sibling = lax.ppermute(give, "slab", [(i, i ^ 1) for i in range(n_slab)])
        mine = keep + sibling
        pieces = lax.all_to_all(mine, "slab", split_axis=0, concat_axis=0, tiled=True)
        pieces = pieces.reshape(n_slab // 2, 2, -1)
        summed = jnp.sum(pieces, axis=0)
        blocks = gathered(summed[None], "slab")
        return blocks.transpose(1, 0, 2).reshape(both.shape)
    pieces = lax.all_to_all(both.reshape(n_slab, -1), "slab", split_axis=0, concat_axis=0, tiled=True)
    summed = jnp.sum(pieces, axis=0, keepdims=True)
    return gathered(summed, "slab").reshape(both.shape)


def tap_sums(products, sign, n_high, n_wide):
    sums = []
    for depth_tap in range(3):
        total = None
        for high_tap in range(3):
            for wide_tap in range(3):
                moved = shifted_cells(
                    products[depth_tap, high_tap, wide_tap],
                    sign * (high_tap - 1),
                    sign * (wide_tap - 1),
                    n_high,
                    n_wide,
                )
                total = moved if total is None else total + moved
        sums.append(total)
    return sums


def on_device(inputs, weight, conv_bias, out_grad):
    n_local, n_depth, n_high, n_wide = inputs.shape
    n_chan = weight.shape[4]
    cells = n_depth * n_high * n_wide
    grad_scale = 1.0 / math.sqrt(cells * lax.axis_size("slab"))

    n_part = lax.axis_size("chan")
    weight_flat = weight.reshape(n_local, 27, n_chan)
    weight_split = weight_flat.reshape(n_local, 27, n_part, n_local).transpose(2, 0, 1, 3)
    in_flat = inputs.reshape(n_local, cells)
    in_copies = jnp.broadcast_to(in_flat[None], (n_part, n_local, cells))
    sent = jnp.concatenate([in_copies, weight_split.reshape(n_part, n_local, 27 * n_local)], axis=2)
    came = lax.all_to_all(sent, "chan", split_axis=0, concat_axis=0, tiled=True)
    in_all = came[:, :, :cells].reshape(n_chan, cells)
    weight_cols = came[:, :, cells:].reshape(n_chan, 27, n_local)

    weight_rows = weight_flat.transpose(1, 0, 2).reshape(27 * n_local, n_chan)
    products = jnp.dot(weight_rows, in_all, preferred_element_type=jnp.float32)
    products = products.reshape(3, 3, 3, n_local, cells)
    fwd = tap_sums(products, 1, n_high, n_wide)
    pre_sum = fwd[1] + from_below(fwd[0], "slab") + from_above(fwd[2], "slab")
    pre_sum = pre_sum + conv_bias.astype(jnp.float32)[:, None]
    activated = jax.nn.silu(pre_sum).astype(jnp.bfloat16).reshape(inputs.shape)
    slope = (out_grad.reshape(n_local, cells).astype(jnp.float32) * silu_grad(pre_sum)).astype(
        jnp.bfloat16
    )

    slope_below = from_below(slope, "slab")
    slope_above = from_above(slope, "slab")
    slope_planes = (slope_above, slope, slope_below)
    slope_moved = jnp.stack(
        [
            shifted_cells(slope_planes[depth_tap], 1 - high_tap, 1 - wide_tap, n_high, n_wide)
            for depth_tap in range(3)
            for high_tap in range(3)
            for wide_tap in range(3)
        ],
        axis=0,
    ).reshape(27 * n_local, cells)
    tap_grad = lax.dot_general(
        slope_moved, in_all, (((1,), (1,)), ((), ())), preferred_element_type=jnp.float32
    )
    kernel_part = tap_grad.reshape(27, n_local, n_chan).transpose(1, 0, 2)
    bias_part = jnp.sum(slope.astype(jnp.float32), axis=1)
    bias_row = jnp.zeros((n_local, 1, n_chan), jnp.float32).at[:, 0, 0].set(bias_part)
    both = jnp.concatenate([kernel_part, bias_row], axis=1)
    slope_all = gathered(slope, "chan")
    both, slope_all = lax.optimization_barrier((both, slope_all))
    total = slab_total(both)
    kernel_total = total[:, :27].reshape(n_local, 3, 3, 3, n_chan) * grad_scale
    bias_total = total[:, 27, 0] * grad_scale

    back = lax.dot_general(
        weight_cols.reshape(n_chan, 27 * n_local),
        slope_all,
        (((0,), (0,)), ((), ())),
        preferred_element_type=jnp.float32,
    )
    back = back.reshape(3, 3, 3, n_local, cells)
    bwd = tap_sums(back, -1, n_high, n_wide)
    back_total = bwd[1] + from_above(bwd[0], "slab") + from_below(bwd[2], "slab")
    input_grad = back_total.astype(jnp.bfloat16).reshape(inputs.shape)
    return (activated, input_grad, kernel_total, bias_total)


def solution(mesh):
    placed = (
        P("chan", "slab", None, None),
        P("chan", None, None, None, None),
        P("chan"),
        P("chan", "slab", None, None),
    )
    return jax.shard_map(
        on_device,
        mesh=mesh,
        in_specs=placed,
        out_specs=(
            P("chan", "slab", None, None),
            P("chan", "slab", None, None),
            P("chan", None, None, None, None),
            P("chan"),
        ),
        check_vma=False,
    )
```

```python
import math

import jax
import jax.numpy as jnp
from jax import lax
from jax.sharding import PartitionSpec as P


def silu_grad(values):
    sig = jax.nn.sigmoid(values)
    return sig * (1.0 + values * (1.0 - sig))


def shifted_cells(values, high_step, wide_step, n_high, n_wide):
    length = values.shape[-1]
    offset = high_step * n_wide + wide_step
    if offset > 0:
        filler = jnp.zeros(values.shape[:-1] + (offset,), values.dtype)
        moved = jnp.concatenate([values[..., offset:], filler], axis=-1)
    elif offset < 0:
        filler = jnp.zeros(values.shape[:-1] + (-offset,), values.dtype)
        moved = jnp.concatenate([filler, values[..., :offset]], axis=-1)
    else:
        moved = values
    position = lax.iota(jnp.int32, length)
    high_index = position // n_wide % n_high + high_step
    wide_index = position % n_wide + wide_step
    valid = (high_index >= 0) & (high_index < n_high) & (wide_index >= 0) & (wide_index < n_wide)
    return jnp.where(valid, moved, jnp.zeros_like(moved))


def from_below(values, axis):
    count = lax.axis_size(axis)
    return lax.ppermute(values, axis, [(i, i + 1) for i in range(count - 1)])


def from_above(values, axis):
    count = lax.axis_size(axis)
    return lax.ppermute(values, axis, [(i + 1, i) for i in range(count - 1)])


def gathered(values, axis):
    count = lax.axis_size(axis)
    copies = jnp.broadcast_to(values[None], (count, *values.shape))
    blocks = lax.all_to_all(copies, axis, split_axis=0, concat_axis=0, tiled=True)
    return blocks.reshape(count * values.shape[0], *values.shape[1:])


REDUCE = "pair"


def slab_total(both):
    n_slab = lax.axis_size("slab")
    if REDUCE == "psum":
        return lax.psum(both, "slab")
    if REDUCE == "rs_ag":
        piece = lax.psum_scatter(both.reshape(n_slab, -1), "slab", scatter_dimension=0, tiled=True)
        return lax.all_gather(piece, "slab", axis=0, tiled=True).reshape(both.shape)
    if REDUCE == "rs_a2a":
        piece = lax.psum_scatter(both.reshape(n_slab, -1), "slab", scatter_dimension=0, tiled=True)
        return gathered(piece, "slab").reshape(both.shape)
    if REDUCE == "pair":
        halves = both.reshape(2, n_slab, -1)
        parity = lax.axis_index("slab") % 2
        keep = jnp.where(parity == 0, halves[0], halves[1])
        give = jnp.where(parity == 0, halves[1], halves[0])
        sibling = lax.ppermute(give, "slab", [(i, i ^ 1) for i in range(n_slab)])
        mine = keep + sibling
        pieces = lax.all_to_all(mine, "slab", split_axis=0, concat_axis=0, tiled=True)
        pieces = pieces.reshape(n_slab // 2, 2, -1)
        summed = jnp.sum(pieces, axis=0)
        sent = summed[jnp.arange(n_slab) % 2]
        own_half = lax.all_to_all(sent, "slab", split_axis=0, concat_axis=0, tiled=True)
        other_half = lax.ppermute(own_half, "slab", [(i, i ^ 1) for i in range(n_slab)])
        full = jnp.where(
            parity == 0,
            jnp.stack([own_half, other_half]),
            jnp.stack([other_half, own_half]),
        )
        return full.reshape(both.shape)
    pieces = lax.all_to_all(both.reshape(n_slab, -1), "slab", split_axis=0, concat_axis=0, tiled=True)
    summed = jnp.sum(pieces, axis=0, keepdims=True)
    return gathered(summed, "slab").reshape(both.shape)


def tap_sums(products, sign, n_high, n_wide):
    sums = []
    for depth_tap in range(3):
        total = None
        for high_tap in range(3):
            for wide_tap in range(3):
                moved = shifted_cells(
                    products[depth_tap, high_tap, wide_tap],
                    sign * (high_tap - 1),
                    sign * (wide_tap - 1),
                    n_high,
                    n_wide,
                )
                total = moved if total is None else total + moved
        sums.append(total)
    return sums


def on_device(inputs, weight, conv_bias, out_grad):
    n_local, n_depth, n_high, n_wide = inputs.shape
    n_chan = weight.shape[4]
    cells = n_depth * n_high * n_wide
    grad_scale = 1.0 / math.sqrt(cells * lax.axis_size("slab"))

    n_part = lax.axis_size("chan")
    weight_flat = weight.reshape(n_local, 27, n_chan)
    weight_split = weight_flat.reshape(n_local, 27, n_part, n_local).transpose(2, 0, 1, 3)
    in_flat = inputs.reshape(n_local, cells)
    in_copies = jnp.broadcast_to(in_flat[None], (n_part, n_local, cells))
    sent = jnp.concatenate([in_copies, weight_split.reshape(n_part, n_local, 27 * n_local)], axis=2)
    came = lax.all_to_all(sent, "chan", split_axis=0, concat_axis=0, tiled=True)
    in_all = came[:, :, :cells].reshape(n_chan, cells)
    weight_cols = came[:, :, cells:].reshape(n_chan, 27, n_local)

    weight_rows = weight_flat.transpose(1, 0, 2).reshape(27 * n_local, n_chan)
    products = jnp.dot(weight_rows, in_all, preferred_element_type=jnp.float32)
    products = products.reshape(3, 3, 3, n_local, cells)
    fwd = tap_sums(products, 1, n_high, n_wide)
    pre_sum = fwd[1] + from_below(fwd[0], "slab") + from_above(fwd[2], "slab")
    pre_sum = pre_sum + conv_bias.astype(jnp.float32)[:, None]
    activated = jax.nn.silu(pre_sum).astype(jnp.bfloat16).reshape(inputs.shape)
    slope = (out_grad.reshape(n_local, cells).astype(jnp.float32) * silu_grad(pre_sum)).astype(
        jnp.bfloat16
    )

    slope_below = from_below(slope, "slab")
    slope_above = from_above(slope, "slab")
    slope_planes = (slope_above, slope, slope_below)
    slope_moved = jnp.stack(
        [
            shifted_cells(slope_planes[depth_tap], 1 - high_tap, 1 - wide_tap, n_high, n_wide)
            for depth_tap in range(3)
            for high_tap in range(3)
            for wide_tap in range(3)
        ],
        axis=0,
    ).reshape(27 * n_local, cells)
    tap_grad = lax.dot_general(
        slope_moved, in_all, (((1,), (1,)), ((), ())), preferred_element_type=jnp.float32
    )
    kernel_part = tap_grad.reshape(27, n_local, n_chan).transpose(1, 0, 2)
    bias_part = jnp.sum(slope.astype(jnp.float32), axis=1)
    bias_row = jnp.zeros((n_local, 1, n_chan), jnp.float32).at[:, 0, 0].set(bias_part)
    both = jnp.concatenate([kernel_part, bias_row], axis=1)
    slope_all = gathered(slope, "chan")
    both, slope_all = lax.optimization_barrier((both, slope_all))
    total = slab_total(both)
    kernel_total = total[:, :27].reshape(n_local, 3, 3, 3, n_chan) * grad_scale
    bias_total = total[:, 27, 0] * grad_scale

    back = lax.dot_general(
        weight_cols.reshape(n_chan, 27 * n_local),
        slope_all,
        (((0,), (0,)), ((), ())),
        preferred_element_type=jnp.float32,
    )
    back = back.reshape(3, 3, 3, n_local, cells)
    bwd = tap_sums(back, -1, n_high, n_wide)
    back_total = bwd[1] + from_above(bwd[0], "slab") + from_below(bwd[2], "slab")
    input_grad = back_total.astype(jnp.bfloat16).reshape(inputs.shape)
    return (activated, input_grad, kernel_total, bias_total)


def solution(mesh):
    placed = (
        P("chan", "slab", None, None),
        P("chan", None, None, None, None),
        P("chan"),
        P("chan", "slab", None, None),
    )
    return jax.shard_map(
        on_device,
        mesh=mesh,
        in_specs=placed,
        out_specs=(
            P("chan", "slab", None, None),
            P("chan", "slab", None, None),
            P("chan", None, None, None, None),
            P("chan"),
        ),
        check_vma=False,
    )
```
